128 devices in a mesh: blk: 2 (over x_lo), tile: 64 (over z, y, x_hi, core).
Axes of the slice: x: 4 (x_hi: 2, x_lo: 2; x = x_hi * 2 + x_lo), y: 4, z: 4, core: 2. Of those that a mesh axis runs over, the one named last changes fastest.
Arguments:
- forward: float32 [2, 1024, 65536], P(None, 'blk', 'tile'), may hold values from -6 to 6
- backward: float32 [2, 1024, 65536], P(None, 'blk', 'tile'), may hold values from -6 to 6
- phase: float32 [64, 1024], P('tile'), may hold values from -3.140625 to 3.140625
- footprint: int32 [16, 64], P('blk', 'tile'), may hold values 0 or 1
- groups: int32 [1024], replicated, may hold values from 0 to 44
Outputs:
- margin: float32 [2, 1024, 1024], P(None, 'blk', 'tile')
- gradient: float32 [64, 1024], P('tile', 'blk')
The draws below stay inside these ranges and needn't reach their ends.
All inputs are finite; a program needn't handle non-finite values. No bound on the sum of `footprint` on one device may be relied on, other than what follows from the above.
Results may differ from the reference program's by a relative error of at most 0.00016.
Values sent between devices are 32-bit elements; how exact they have to be, the bound alone decides.
No kernel may reach another device: no remote copies, remote signals or barrier semaphores. Data moves between devices by JAX's collectives and lax.ppermute only.
A program may use at most 320 MiB of HBM per device.

```python
import math
import jax
import jax.numpy as jnp
from jax import lax

MODES = 1024
WIDTH = 1024
ROWS_DEV = 1
BLOCK = 64
NGROUP = 45
PIX_DEV = 1024
TILES = 64
ROWS = 64
PIXELS = 65536
MODE_BLOCKS = 16


def touch_ends(result, rng, least, high):
    extent = result.shape
    spot = [jax.random.randint(jax.random.fold_in(rng, axis), (), 0, extent[axis]) for axis in range(len(extent))]
    result = result.at[tuple(spot)].set(least)
    longest = extent.index(max(extent))
    spot[longest] = (spot[longest] + 1) % extent[longest]
    return result.at[tuple(spot)].set(high)


def steps_of(own_key, extent, shards, smallest, high):
    loudness, own = 1.0, jax.random.fold_in(own_key, 6)
    for dim, shards_of in shards:
        steps = jnp.exp(jax.random.uniform(jax.random.fold_in(own, dim), (shards_of,), jnp.float32, smallest / len(shards), high / len(shards)))
        loudness = loudness * jnp.repeat(steps, extent[dim] // shards_of).reshape([-1 if axis == dim else 1 for axis in range(len(extent))])
    return loudness


def centred(own_key, shape, deviation, most, shards=(), kind=jnp.bfloat16):
    factor_of = steps_of(own_key, shape, shards, -0.22, 0.18) if shards else 1.0
    result = jax.random.normal(own_key, shape, jnp.float32) * deviation * factor_of
    return jnp.minimum(jnp.maximum(result, -most), most).astype(kind)


def setup_inputs(seed: int = 0) -> dict:
    splits = jax.random.split(jax.random.key(seed), 6)
    forward = centred(splits[0], (2, MODES, PIXELS), 1.0, 6.0, ((1, 2), (2, 64)), jnp.float32)
    backward = centred(splits[1], (2, MODES, PIXELS), 1.0, 6.0, ((1, 2), (2, 64)), jnp.float32)
    phase = jnp.clip(jax.random.uniform(splits[2], (ROWS, WIDTH), jnp.float32, -3.140625, 3.140625), -3.140625, 3.140625)
    footprint = touch_ends((jax.random.randint(splits[3], (MODE_BLOCKS, TILES), 0, 4) < 3).astype(jnp.int32), jax.random.fold_in(splits[3], 1), 0, 1)
    groups = touch_ends(jax.random.randint(splits[4], (MODES,), 0, NGROUP), jax.random.fold_in(splits[4], 1), 0, NGROUP - 1).astype(jnp.int32)
    return dict(forward=forward, backward=backward, phase=phase, footprint=footprint, groups=groups)


highest = lax.Precision.HIGHEST
cross_weight = 0.05

def contract_pixels(left_fields, right_fields):
    return lax.dot_general(left_fields, right_fields, (((1,), (1,)), ((), ())), precision=highest, preferred_element_type=jnp.float32)

def contract_modes(left_fields, right_fields):
    return lax.dot_general(left_fields, right_fields, (((0,), (0,)), ((), ())), precision=highest, preferred_element_type=jnp.float32)

def reference(forward, backward, phase, footprint, groups):
    gate_full = footprint.astype(jnp.float32)
    inverse_root = 1.0 / math.sqrt(PIXELS)

    def tile_fields(tile_index):
        forward_tile = lax.dynamic_slice_in_dim(forward, tile_index * PIX_DEV, PIX_DEV, 2)
        backward_tile = lax.dynamic_slice_in_dim(backward, tile_index * PIX_DEV, PIX_DEV, 2)
        phase_tile = lax.dynamic_slice_in_dim(phase, tile_index * ROWS_DEV, ROWS_DEV, 0).reshape(PIX_DEV)
        gate_rows = jnp.repeat(lax.dynamic_slice_in_dim(gate_full, tile_index, 1, 1)[:, 0], BLOCK)
        masked = backward_tile * gate_rows[None, :, None]
        phase_cos = jnp.cos(phase_tile)
        phase_sin = jnp.sin(phase_tile)
        shifted_re = forward_tile[0] * phase_cos - forward_tile[1] * phase_sin
        shifted_im = forward_tile[0] * phase_sin + forward_tile[1] * phase_cos
        return (masked, shifted_re, shifted_im)

    def add_tile(carry, tile_index):
        masked, shifted_re, shifted_im = tile_fields(tile_index)
        real_part = contract_pixels(masked[0], shifted_re) + contract_pixels(masked[1], shifted_im)
        imag_part = contract_pixels(masked[0], shifted_im) - contract_pixels(masked[1], shifted_re)
        return ((carry[0] + real_part, carry[1] + imag_part), None)
    zero_matrix = jnp.zeros((MODES, MODES), jnp.float32)
    tile_range = jnp.arange(TILES, dtype=jnp.int32)
    (sum_re, sum_im), _ = lax.scan(add_tile, (zero_matrix, zero_matrix), tile_range)
    margin_re = sum_re * inverse_root
    margin_im = sum_im * inverse_root
    same_group = groups[:, None] == groups[None, :]
    weights = jnp.where(same_group, 1.0, -cross_weight).astype(jnp.float32)
    coupled_re = weights * margin_re
    coupled_im = weights * margin_im
    grad_scale = 0.25 / math.sqrt(MODES)

    def grad_tile(tile_index):
        masked, shifted_re, shifted_im = tile_fields(tile_index)
        reply_re = contract_modes(coupled_re, masked[0]) - contract_modes(coupled_im, masked[1])
        reply_im = contract_modes(coupled_re, masked[1]) + contract_modes(coupled_im, masked[0])
        return grad_scale * lax.optimization_barrier(jnp.sum(shifted_im * reply_re - shifted_re * reply_im, axis=0))
    gradient = lax.map(grad_tile, tile_range).reshape(ROWS, WIDTH)
    return (jnp.stack([margin_re, margin_im]), gradient)
```

```python
import math

import jax
import numpy as np
import jax.numpy as jnp
from jax import lax
from jax.sharding import PartitionSpec as P

MODES = 1024
BLOCK = 64


TILE = ("z", "y", "xh", "core")
highest = lax.Precision.HIGHEST
cross_weight = 0.05


def pair_margin(left_fields, right_fields):
    left_count = left_fields.shape[1]
    right_count = right_fields.shape[1]
    stacked = lax.dot_general(
        left_fields.reshape(2 * left_count, -1),
        right_fields.reshape(2 * right_count, -1),
        (((1,), (1,)), ((), ())),
        precision=highest,
        preferred_element_type=jnp.float32,
    )
    real_part = stacked[:left_count, :right_count] + stacked[left_count:, right_count:]
    imag_part = stacked[:left_count, right_count:] - stacked[left_count:, :right_count]
    return jnp.stack([real_part, imag_part])


def response(coupled, fields):
    source_count = coupled.shape[1]
    target_count = coupled.shape[2]
    mixing = jnp.stack(
        [
            jnp.concatenate([coupled[0], -coupled[1]], 0),
            jnp.concatenate([coupled[1], coupled[0]], 0),
        ],
        axis=2,
    ).reshape(2 * source_count, 2 * target_count)
    product = lax.dot_general(
        mixing,
        fields.reshape(2 * source_count, -1),
        (((0,), (0,)), ((), ())),
        precision=highest,
        preferred_element_type=jnp.float32,
    )
    return product.reshape(target_count, 2, -1)


def margin_rows(masked, portion):
    return pair_margin(masked, portion)


def response_rows(coupled_rows, masked):
    return response(coupled_rows, masked)


def tile_sum(values):
    rows = values.reshape(-1, values.shape[-1])
    for axes in ("core", ("z", "y"), "xh"):
        rows = lax.psum_scatter(rows, axes, scatter_dimension=0, tiled=True)
    for axes in ("xh", ("z", "y"), "core"):
        rows = lax.all_gather(rows, axes, axis=0, tiled=True)
    return rows.reshape(values.shape)


def body(forward, backward, phase, footprint, groups):
    local_modes = backward.shape[1]
    pixel_count = backward.shape[2]
    rows_here, width_here = phase.shape
    phase_cos = jnp.cos(phase).reshape(pixel_count)
    phase_sin = jnp.sin(phase).reshape(pixel_count)
    shifted = jnp.stack(
        [
            forward[0] * phase_cos - forward[1] * phase_sin,
            forward[0] * phase_sin + forward[1] * phase_cos,
        ]
    )
    tile_count = lax.axis_size(TILE)
    inverse_root = 1.0 / math.sqrt(pixel_count * tile_count)
    grad_scale = 0.25 / math.sqrt(MODES)
    column_share = MODES // tile_count
    tile_offset = lax.axis_index(TILE) * column_share
    mode_offset = lax.axis_index("blk") * local_modes
    row_gate = jnp.repeat(footprint[:, 0].astype(jnp.float32), BLOCK)
    masked = backward * row_gate[None, :, None]
    block_values = margin_rows(masked, lax.all_gather(shifted, "blk", axis=1, tiled=True))
    margin_full = tile_sum(block_values) * inverse_root
    margin_out = lax.dynamic_slice_in_dim(margin_full, tile_offset, column_share, 2)
    own_groups = lax.dynamic_slice_in_dim(groups, mode_offset, local_modes)
    weights = jnp.where(own_groups[:, None] == groups[None, :], 1.0, -cross_weight).astype(
        jnp.float32
    )
    coupled = margin_full * weights[None]
    portion = lax.all_gather(shifted, "blk", axis=1, tiled=True)
    reply = response_rows(coupled, masked)
    local_sum = jnp.sum(portion[1] * reply[:, 0] - portion[0] * reply[:, 1], axis=0)
    gradient = (
        lax.psum_scatter(
            local_sum.reshape(rows_here, width_here), "blk", scatter_dimension=1, tiled=True
        )
        * grad_scale
    )
    return (margin_out, gradient)


def fine_mesh(mesh):
    devices = np.asarray(mesh.devices)
    blk, tile = devices.shape
    return jax.sharding.Mesh(devices.reshape(blk, 4, tile // 16, 2, 2), ("blk",) + TILE)


def solution(mesh):
    mesh = fine_mesh(mesh)
    placed = (
        P(None, "blk", TILE),
        P(None, "blk", TILE),
        P(TILE, None),
        P("blk", TILE),
        P(),
    )
    return jax.shard_map(
        body,
        mesh=mesh,
        in_specs=placed,
        out_specs=(P(None, "blk", TILE), P(TILE, "blk")),
        check_vma=False,
    )
```

```python
import math

import jax
import jax.numpy as jnp
import numpy as np
from jax import lax
from jax.sharding import PartitionSpec as P

MODES = 1024
BLOCK = 64

TILE = ("z", "y", "xh", "core")
STAGES = (("core", 2), ("z", 4), ("y", 4), ("xh", 2))
highest = lax.Precision.HIGHEST
cross_weight = 0.05


def shift_to(x, axis, size, step):
    return lax.ppermute(x, axis, [(j, (j + step) % size) for j in range(size)])


def scatter_rows(x, axis, size):
    me = lax.axis_index(axis)
    part = x.shape[0] // size
    total = lax.dynamic_slice_in_dim(x, me * part, part, 0)
    for step in range(1, size):
        send = lax.dynamic_slice_in_dim(x, ((me + step) % size) * part, part, 0)
        total = total + shift_to(send, axis, size, step)
    return total


def gather_rows(x, axis, size):
    me = lax.axis_index(axis)
    part = x.shape[0]
    out = jnp.zeros((size * part,) + x.shape[1:], x.dtype)
    out = lax.dynamic_update_slice_in_dim(out, x, me * part, 0)
    for step in range(1, size):
        got = shift_to(x, axis, size, step)
        out = lax.dynamic_update_slice_in_dim(out, got, ((me + size - step) % size) * part, 0)
    return out


def tile_sum(values):
    rows = values.reshape(-1, values.shape[-1])
    for axis, size in STAGES:
        rows = scatter_rows(rows, axis, size)
    for axis, size in reversed(STAGES):
        rows = gather_rows(rows, axis, size)
    return rows.reshape(values.shape)


def pair_margin(fields, portion):
    count = portion.shape[1]
    stacked = lax.dot_general(
        fields,
        portion.reshape(2 * count, -1),
        (((1,), (1,)), ((), ())),
        precision=highest,
        preferred_element_type=jnp.float32,
    )
    half = fields.shape[0] // 2
    real_part = stacked[:half, :count] + stacked[half:, count:]
    imag_part = stacked[:half, count:] - stacked[half:, :count]
    return jnp.stack([real_part, imag_part])


def half_gradient(coupled, fields, portion):
    mixing = jnp.concatenate(
        [
            jnp.concatenate([coupled[0], coupled[1]], 1),
            jnp.concatenate([-coupled[1], coupled[0]], 1),
        ],
        0,
    )
    reply = lax.dot_general(
        mixing,
        fields,
        (((0,), (0,)), ((), ())),
        precision=highest,
        preferred_element_type=jnp.float32,
    ).reshape(2, portion.shape[1], -1)
    return jnp.sum(portion[1] * reply[0] - portion[0] * reply[1], axis=0)


def body(forward, backward, phase, footprint, groups):
    local_modes = backward.shape[1]
    pixel_count = backward.shape[2]
    phase_cos = jnp.cos(phase).reshape(pixel_count)
    phase_sin = jnp.sin(phase).reshape(pixel_count)
    shifted = jnp.stack(
        [
            forward[0] * phase_cos - forward[1] * phase_sin,
            forward[0] * phase_sin + forward[1] * phase_cos,
        ]
    )
    other = shift_to(shifted, "blk", 2, 1)
    tile_count = lax.axis_size(TILE)
    inverse_root = 1.0 / math.sqrt(pixel_count * tile_count)
    grad_scale = 0.25 / math.sqrt(MODES)
    column_share = MODES // tile_count
    me = lax.axis_index("blk")
    row_gate = jnp.repeat(footprint[:, 0].astype(jnp.float32), BLOCK)
    masked = backward * row_gate[None, :, None]
    fields = masked.reshape(2 * local_modes, pixel_count)

    own_groups = lax.dynamic_slice_in_dim(groups, me * local_modes, local_modes)
    other_groups = lax.dynamic_slice_in_dim(groups, (1 - me) * local_modes, local_modes)

    def half(portion, column_groups):
        margin_half = tile_sum(pair_margin(fields, portion)) * inverse_root
        weights = jnp.where(own_groups[:, None] == column_groups[None, :], 1.0, -cross_weight)
        coupled = margin_half * weights.astype(jnp.float32)[None]
        return margin_half, half_gradient(coupled, fields, portion)

    margin_own, sum_own = half(shifted, own_groups)
    margin_other, sum_other = half(other, other_groups)

    column = lax.axis_index(TILE) * column_share
    offset = column % local_modes
    margin_out = jnp.where(
        column // local_modes == me,
        lax.dynamic_slice_in_dim(margin_own, offset, column_share, 2),
        lax.dynamic_slice_in_dim(margin_other, offset, column_share, 2),
    )

    local_sum = (sum_own + sum_other) * grad_scale
    half_width = pixel_count // 2
    keep = lax.dynamic_slice_in_dim(local_sum, me * half_width, half_width, 0)
    send = lax.dynamic_slice_in_dim(local_sum, (1 - me) * half_width, half_width, 0)
    gradient = keep + shift_to(send, "blk", 2, 1)
    return (margin_out, gradient.reshape(phase.shape[0], half_width))


def fine_mesh(mesh):
    devices = np.asarray(mesh.devices)
    blk, tile = devices.shape
    return jax.sharding.Mesh(devices.reshape(blk, 4, tile // 16, 2, 2), ("blk",) + TILE)


def solution(mesh):
    mesh = fine_mesh(mesh)
    placed = (
        P(None, "blk", TILE),
        P(None, "blk", TILE),
        P(TILE, None),
        P("blk", TILE),
        P(),
    )
    return jax.shard_map(
        body,
        mesh=mesh,
        in_specs=placed,
        out_specs=(P(None, "blk", TILE), P(TILE, "blk")),
        check_vma=False,
    )
```

```python
import math

import jax
import jax.numpy as jnp
import numpy as np
from jax import lax
from jax.sharding import PartitionSpec as P


MODES = 1024
BLOCK = 64

TILE = ("z", "y", "xh", "core")
STAGES = (("core", 2), ("z", 4), ("y", 4), ("xh", 2))
highest = lax.Precision.HIGH
cross_weight = 0.05


def shift_to(x, axis, size, step):
    return lax.ppermute(x, axis, [(j, (j + step) % size) for j in range(size)])


def scatter_rows(x, axis, size):
    me = lax.axis_index(axis)
    part = x.shape[0] // size
    total = lax.dynamic_slice_in_dim(x, me * part, part, 0)
    for step in range(1, size):
        send = lax.dynamic_slice_in_dim(x, ((me + step) % size) * part, part, 0)
        total = total + shift_to(send, axis, size, step)
    return total


def gather_rows(x, axis, size):
    me = lax.axis_index(axis)
    part = x.shape[0]
    out = jnp.zeros((size * part,) + x.shape[1:], x.dtype)
    out = lax.dynamic_update_slice_in_dim(out, x, me * part, 0)
    for step in range(1, size):
        got = shift_to(x, axis, size, step)
        out = lax.dynamic_update_slice_in_dim(out, got, ((me + size - step) % size) * part, 0)
    return out


def tile_sum(values):
    rows = values.reshape(-1, values.shape[-1])
    for axis, size in STAGES:
        rows = scatter_rows(rows, axis, size)
    for axis, size in reversed(STAGES):
        rows = gather_rows(rows, axis, size)
    return rows.reshape(values.shape)


def pair_margin(fields, portion):
    count = portion.shape[1]
    stacked = lax.dot_general(
        fields,
        portion.reshape(2 * count, -1),
        (((1,), (1,)), ((), ())),
        precision=highest,
        preferred_element_type=jnp.float32,
    )
    half = fields.shape[0] // 2
    real_part = stacked[:half, :count] + stacked[half:, count:]
    imag_part = stacked[:half, count:] - stacked[half:, :count]
    return jnp.stack([real_part, imag_part])


def half_gradient(coupled, fields, portion):
    mixing = jnp.concatenate(
        [
            jnp.concatenate([coupled[0], coupled[1]], 1),
            jnp.concatenate([-coupled[1], coupled[0]], 1),
        ],
        0,
    )
    reply = lax.dot_general(
        mixing,
        fields,
        (((0,), (0,)), ((), ())),
        precision=highest,
        preferred_element_type=jnp.float32,
    ).reshape(2, portion.shape[1], -1)
    return jnp.sum(portion[1] * reply[0] - portion[0] * reply[1], axis=0)


def layer(forward, backward, phase, footprint, groups):
    local_modes = backward.shape[1]
    pixel_count = backward.shape[2]
    phase_cos = jnp.cos(phase).reshape(pixel_count)
    phase_sin = jnp.sin(phase).reshape(pixel_count)
    shifted = jnp.stack(
        [
            forward[0] * phase_cos - forward[1] * phase_sin,
            forward[0] * phase_sin + forward[1] * phase_cos,
        ]
    )
    other = shift_to(shifted, "blk", 2, 1)
    tile_count = lax.axis_size(TILE)
    inverse_root = 1.0 / math.sqrt(pixel_count * tile_count)
    grad_scale = 0.25 / math.sqrt(MODES)
    column_share = MODES // tile_count
    me = lax.axis_index("blk")
    row_gate = jnp.repeat(footprint[:, 0].astype(jnp.float32), BLOCK)
    masked = backward * row_gate[None, :, None]
    fields = masked.reshape(2 * local_modes, pixel_count)

    own_groups = lax.dynamic_slice_in_dim(groups, me * local_modes, local_modes)
    other_groups = lax.dynamic_slice_in_dim(groups, (1 - me) * local_modes, local_modes)

    def half(portion, column_groups):
        margin_half = tile_sum(pair_margin(fields, portion)) * inverse_root
        weights = jnp.where(own_groups[:, None] == column_groups[None, :], 1.0, -cross_weight)
        coupled = margin_half * weights.astype(jnp.float32)[None]
        return margin_half, half_gradient(coupled, fields, portion)

    margin_own, sum_own = half(shifted, own_groups)
    other, sum_own = lax.optimization_barrier((other, sum_own))
    margin_other, sum_other = half(other, other_groups)

    column = lax.axis_index(TILE) * column_share
    offset = column % local_modes
    margin_out = jnp.where(
        column // local_modes == me,
        lax.dynamic_slice_in_dim(margin_own, offset, column_share, 2),
        lax.dynamic_slice_in_dim(margin_other, offset, column_share, 2),
    )

    local_sum = (sum_own + sum_other) * grad_scale
    half_width = pixel_count // 2
    keep = lax.dynamic_slice_in_dim(local_sum, me * half_width, half_width, 0)
    send = lax.dynamic_slice_in_dim(local_sum, (1 - me) * half_width, half_width, 0)
    gradient = keep + shift_to(send, "blk", 2, 1)
    return (margin_out, gradient.reshape(phase.shape[0], half_width))


def fine_mesh(mesh):
    devices = np.asarray(mesh.devices)
    blk, tile = devices.shape
    return jax.sharding.Mesh(devices.reshape(blk, 4, tile // 16, 2, 2), ("blk",) + TILE)


def solution(mesh):
    mesh = fine_mesh(mesh)
    placed = (
        P(None, "blk", TILE),
        P(None, "blk", TILE),
        P(TILE, None),
        P("blk", TILE),
        P(),
    )
    return jax.shard_map(
        layer,
        mesh=mesh,
        in_specs=placed,
        out_specs=(P(None, "blk", TILE), P(TILE, "blk")),
        check_vma=False,
    )
```

```python
import math

import jax
import jax.numpy as jnp
import numpy as np
from jax import lax
from jax.sharding import PartitionSpec as P


MODES = 1024
BLOCK = 64

TILE = ("z", "y", "xh", "core")
SCATTERED = (("core", 2), ("z", 4))
REDUCED = (("y", 4), ("xh", 2))
highest = lax.Precision.HIGH
cross_weight = 0.05


def shift_to(x, axis, size, step):
    return lax.ppermute(x, axis, [(j, (j + step) % size) for j in range(size)])


def scatter_rows(x, axis, size):
    me = lax.axis_index(axis)
    part = x.shape[0] // size
    total = lax.dynamic_slice_in_dim(x, me * part, part, 0)
    for step in range(1, size):
        send = lax.dynamic_slice_in_dim(x, ((me + step) % size) * part, part, 0)
        total = total + shift_to(send, axis, size, step)
    return total


def gather_rows(x, axis, size):
    me = lax.axis_index(axis)
    part = x.shape[0]
    out = jnp.zeros((size * part,) + x.shape[1:], x.dtype)
    out = lax.dynamic_update_slice_in_dim(out, x, me * part, 0)
    for step in range(1, size):
        got = shift_to(x, axis, size, step)
        out = lax.dynamic_update_slice_in_dim(out, got, ((me + size - step) % size) * part, 0)
    return out


def reduce_rows(x, axis, size):
    got = [shift_to(x, axis, size, step) for step in range(1, size)]
    for part in got:
        x = x + part
    return x


def tile_sum(values):
    rows = values.reshape(-1, values.shape[-1])
    for axis, size in SCATTERED:
        rows = scatter_rows(rows, axis, size)
    for axis, size in REDUCED:
        rows = reduce_rows(rows, axis, size)
    for axis, size in reversed(SCATTERED):
        rows = gather_rows(rows, axis, size)
    return rows.reshape(values.shape)


def pair_margin(fields, portion):
    count = portion.shape[1]
    stacked = lax.dot_general(
        fields,
        portion.reshape(2 * count, -1),
        (((1,), (1,)), ((), ())),
        precision=highest,
        preferred_element_type=jnp.float32,
    )
    half = fields.shape[0] // 2
    real_part = stacked[:half, :count] + stacked[half:, count:]
    imag_part = stacked[:half, count:] - stacked[half:, :count]
    return jnp.stack([real_part, imag_part])


def half_gradient(coupled, fields, portion):
    mixing = jnp.concatenate(
        [
            jnp.concatenate([coupled[0], coupled[1]], 1),
            jnp.concatenate([-coupled[1], coupled[0]], 1),
        ],
        0,
    )
    reply = lax.dot_general(
        mixing,
        fields,
        (((0,), (0,)), ((), ())),
        precision=highest,
        preferred_element_type=jnp.float32,
    ).reshape(2, portion.shape[1], -1)
    return jnp.sum(portion[1] * reply[0] - portion[0] * reply[1], axis=0)


def layer(forward, backward, phase, footprint, groups):
    local_modes = backward.shape[1]
    pixel_count = backward.shape[2]
    phase_cos = jnp.cos(phase).reshape(pixel_count)
    phase_sin = jnp.sin(phase).reshape(pixel_count)
    shifted = jnp.stack(
        [
            forward[0] * phase_cos - forward[1] * phase_sin,
            forward[0] * phase_sin + forward[1] * phase_cos,
        ]
    )
    split = local_modes // 2
    other_first = shift_to(shifted[:, :split], "blk", 2, 1)
    other_second = shift_to(shifted[:, split:], "blk", 2, 1)
    tile_count = lax.axis_size(TILE)
    inverse_root = 1.0 / math.sqrt(pixel_count * tile_count)
    grad_scale = 0.25 / math.sqrt(MODES)
    column_share = MODES // tile_count
    me = lax.axis_index("blk")
    row_gate = jnp.repeat(footprint[:, 0].astype(jnp.float32), BLOCK)
    masked = backward * row_gate[None, :, None]
    fields = masked.reshape(2 * local_modes, pixel_count)

    own_groups = lax.dynamic_slice_in_dim(groups, me * local_modes, local_modes)
    other_groups = lax.dynamic_slice_in_dim(groups, (1 - me) * local_modes, local_modes)

    def half(portion, column_groups):
        margin_half = pair_margin(fields, portion)
        margin_half = tile_sum(margin_half) * inverse_root
        weights = jnp.where(own_groups[:, None] == column_groups[None, :], 1.0, -cross_weight)
        coupled = margin_half * weights.astype(jnp.float32)[None]
        return margin_half, half_gradient(coupled, fields, portion)

    margin_own, sum_own = half(shifted, own_groups)
    other_first, other_second, sum_own = lax.optimization_barrier((other_first, other_second, sum_own))
    other = jnp.concatenate([other_first, other_second], 1)
    margin_other, sum_other = half(other, other_groups)

    column = lax.axis_index(TILE) * column_share
    offset = column % local_modes
    margin_out = jnp.where(
        column // local_modes == me,
        lax.dynamic_slice_in_dim(margin_own, offset, column_share, 2),
        lax.dynamic_slice_in_dim(margin_other, offset, column_share, 2),
    )

    local_sum = (sum_own + sum_other) * grad_scale
    half_width = pixel_count // 2
    keep = lax.dynamic_slice_in_dim(local_sum, me * half_width, half_width, 0)
    send = lax.dynamic_slice_in_dim(local_sum, (1 - me) * half_width, half_width, 0)
    gradient = keep + shift_to(send, "blk", 2, 1)
    return (margin_out, gradient.reshape(phase.shape[0], half_width))


def fine_mesh(mesh):
    devices = np.asarray(mesh.devices)
    blk, tile = devices.shape
    return jax.sharding.Mesh(devices.reshape(blk, 4, tile // 16, 2, 2), ("blk",) + TILE)


def solution(mesh):
    mesh = fine_mesh(mesh)
    placed = (
        P(None, "blk", TILE),
        P(None, "blk", TILE),
        P(TILE, None),
        P("blk", TILE),
        P(),
    )
    return jax.shard_map(
        layer,
        mesh=mesh,
        in_specs=placed,
        out_specs=(P(None, "blk", TILE), P(TILE, "blk")),
        check_vma=False,
    )
```

```python
import math

import jax
import jax.numpy as jnp
import numpy as np
from jax import lax
from jax.sharding import PartitionSpec as P


MODES = 1024
BLOCK = 64

TILE = ("z", "y", "xh", "core")
SCATTERED = (("core", 2), ("z", 4))
REDUCED = (("y", 4), ("xh", 2))
highest = lax.Precision.HIGH
cross_weight = 0.05


def shift_to(x, axis, size, step):
    return lax.ppermute(x, axis, [(j, (j + step) % size) for j in range(size)])


def scatter_rows(x, axis, size):
    me = lax.axis_index(axis)
    part = x.shape[0] // size
    total = lax.dynamic_slice_in_dim(x, me * part, part, 0)
    for step in range(1, size):
        send = lax.dynamic_slice_in_dim(x, ((me + step) % size) * part, part, 0)
        total = total + shift_to(send, axis, size, step)
    return total


def gather_rows(x, axis, size):
    me = lax.axis_index(axis)
    part = x.shape[0]
    out = jnp.zeros((size * part,) + x.shape[1:], x.dtype)
    out = lax.dynamic_update_slice_in_dim(out, x, me * part, 0)
    for step in range(1, size):
        got = shift_to(x, axis, size, step)
        out = lax.dynamic_update_slice_in_dim(out, got, ((me + size - step) % size) * part, 0)
    return out


def reduce_rows(x, axis, size):
    got = [shift_to(x, axis, size, step) for step in range(1, size)]
    for part in got:
        x = x + part
    return x


def tile_sum(values):
    rows = values.reshape(-1, values.shape[-1])
    for axis, size in SCATTERED:
        rows = scatter_rows(rows, axis, size)
    for axis, size in REDUCED:
        rows = reduce_rows(rows, axis, size)
    for axis, size in reversed(SCATTERED):
        rows = gather_rows(rows, axis, size)
    return rows.reshape(values.shape)


def pair_margin(fields, portion):
    count = portion.shape[1]
    stacked = lax.dot_general(
        fields,
        portion.reshape(2 * count, -1),
        (((1,), (1,)), ((), ())),
        precision=highest,
        preferred_element_type=jnp.float32,
    )
    half = fields.shape[0] // 2
    real_part = stacked[:half, :count] + stacked[half:, count:]
    imag_part = stacked[:half, count:] - stacked[half:, :count]
    return jnp.stack([real_part, imag_part])


def half_gradient(coupled, fields, portions):
    mixing = jnp.concatenate(
        [
            jnp.concatenate([coupled[0], coupled[1]], 1),
            jnp.concatenate([-coupled[1], coupled[0]], 1),
        ],
        0,
    )
    reply = lax.dot_general(
        mixing,
        fields,
        (((0,), (0,)), ((), ())),
        precision=highest,
        preferred_element_type=jnp.float32,
    ).reshape(2, coupled.shape[2], -1)
    total = 0.0
    start = 0
    for part in portions:
        count = part.shape[1]
        piece = reply[:, start : start + count]
        total = total + jnp.sum(part[1] * piece[0] - part[0] * piece[1], axis=0)
        start += count
    return total


def layer(forward, backward, phase, footprint, groups):
    local_modes = backward.shape[1]
    pixel_count = backward.shape[2]
    phase_cos = jnp.cos(phase).reshape(pixel_count)
    phase_sin = jnp.sin(phase).reshape(pixel_count)

    def rotate(raw, cos=phase_cos, sin=phase_sin):
        return jnp.stack([raw[0] * cos - raw[1] * sin, raw[0] * sin + raw[1] * cos])

    split = local_modes // 2
    raw_first = shift_to(forward[:, :split], "blk", 2, 1)
    raw_second = shift_to(forward[:, split:], "blk", 2, 1)
    shifted = rotate(forward)
    tile_count = lax.axis_size(TILE)
    inverse_root = 1.0 / math.sqrt(pixel_count * tile_count)
    grad_scale = 0.25 / math.sqrt(MODES)
    column_share = MODES // tile_count
    me = lax.axis_index("blk")
    row_gate = jnp.repeat(footprint[:, 0].astype(jnp.float32), BLOCK)
    masked = backward * row_gate[None, :, None]
    fields = masked.reshape(2 * local_modes, pixel_count)

    own_groups = lax.dynamic_slice_in_dim(groups, me * local_modes, local_modes)
    other_groups = lax.dynamic_slice_in_dim(groups, (1 - me) * local_modes, local_modes)

    def coupled_of(margin_half, column_groups):
        weights = jnp.where(own_groups[:, None] == column_groups[None, :], 1.0, -cross_weight)
        return margin_half * weights.astype(jnp.float32)[None]

    own_block = pair_margin(fields, shifted)
    margin_own = tile_sum(own_block) * inverse_root
    sum_own = half_gradient(coupled_of(margin_own, own_groups), fields, [shifted])
    other_first = rotate(raw_first)
    first_block = pair_margin(fields, other_first)
    raw_second, late_cos, late_sin = lax.optimization_barrier((raw_second, phase_cos, phase_sin))
    other_second = rotate(raw_second, late_cos, late_sin)
    other_blocks = jnp.stack([first_block, pair_margin(fields, other_second)])
    margin_other = tile_sum(other_blocks) * inverse_root
    sum_other = 0.0
    for index, portion in enumerate((other_first, other_second)):
        column_groups = lax.dynamic_slice_in_dim(other_groups, index * split, split)
        coupled = coupled_of(margin_other[index], column_groups)
        sum_other = sum_other + half_gradient(coupled, fields, [portion])

    column = lax.axis_index(TILE) * column_share
    offset = column % local_modes
    other_rows = lax.dynamic_index_in_dim(margin_other, offset // split, 0, keepdims=False)
    margin_out = jnp.where(
        column // local_modes == me,
        lax.dynamic_slice_in_dim(margin_own, offset, column_share, 2),
        lax.dynamic_slice_in_dim(other_rows, offset % split, column_share, 2),
    )

    local_sum = (sum_own + sum_other) * grad_scale
    half_width = pixel_count // 2
    keep = lax.dynamic_slice_in_dim(local_sum, me * half_width, half_width, 0)
    send = lax.dynamic_slice_in_dim(local_sum, (1 - me) * half_width, half_width, 0)
    gradient = keep + shift_to(send, "blk", 2, 1)
    return (margin_out, gradient.reshape(phase.shape[0], half_width))


def fine_mesh(mesh):
    devices = np.asarray(mesh.devices)
    blk, tile = devices.shape
    return jax.sharding.Mesh(devices.reshape(blk, 4, tile // 16, 2, 2), ("blk",) + TILE)


def solution(mesh):
    mesh = fine_mesh(mesh)
    placed = (
        P(None, "blk", TILE),
        P(None, "blk", TILE),
        P(TILE, None),
        P("blk", TILE),
        P(),
    )
    return jax.shard_map(
        layer,
        mesh=mesh,
        in_specs=placed,
        out_specs=(P(None, "blk", TILE), P(TILE, "blk")),
        check_vma=False,
    )
```

```python
import math

import jax
import jax.numpy as jnp
import numpy as np
from jax import lax
from jax.sharding import PartitionSpec as P


MODES = 1024
BLOCK = 64

TILE = ("z", "y", "xh", "core")
SCATTERED = (("core", 2), ("z", 4))
highest = lax.Precision.HIGH
cross_weight = 0.05


def shift_to(x, axis, size, step):
    return lax.ppermute(x, axis, [(j, (j + step) % size) for j in range(size)])


def scatter_rows(x, axis, size):
    me = lax.axis_index(axis)
    part = x.shape[0] // size
    total = lax.dynamic_slice_in_dim(x, me * part, part, 0)
    for step in range(1, size):
        send = lax.dynamic_slice_in_dim(x, ((me + step) % size) * part, part, 0)
        total = total + shift_to(send, axis, size, step)
    return total


def gather_rows(x, axis, size):
    me = lax.axis_index(axis)
    part = x.shape[0]
    out = jnp.zeros((size * part,) + x.shape[1:], x.dtype)
    out = lax.dynamic_update_slice_in_dim(out, x, me * part, 0)
    for step in range(1, size):
        got = shift_to(x, axis, size, step)
        out = lax.dynamic_update_slice_in_dim(out, got, ((me + size - step) % size) * part, 0)
    return out


def reduce_rows(x, axis, size):
    got = [shift_to(x, axis, size, step) for step in range(1, size)]
    for part in got:
        x = x + part
    return x


def tile_front(rows):
    for axis, size in SCATTERED:
        rows = scatter_rows(rows, axis, size)
    return reduce_rows(rows, "y", 4)


def tile_back(rows):
    rows = reduce_rows(rows, "xh", 2)
    for axis, size in reversed(SCATTERED):
        rows = gather_rows(rows, axis, size)
    return rows


def tile_sum(values):
    rows = values.reshape(-1, values.shape[-1])
    return tile_back(tile_front(rows)).reshape(values.shape)


def pair_margin(fields, portion):
    count = portion.shape[1]
    stacked = lax.dot_general(
        fields,
        portion.reshape(2 * count, -1),
        (((1,), (1,)), ((), ())),
        precision=highest,
        preferred_element_type=jnp.float32,
    )
    half = fields.shape[0] // 2
    real_part = stacked[:half, :count] + stacked[half:, count:]
    imag_part = stacked[:half, count:] - stacked[half:, :count]
    return jnp.stack([real_part, imag_part])


def half_gradient(coupled, fields, portions):
    mixing = jnp.concatenate(
        [
            jnp.concatenate([coupled[0], coupled[1]], 1),
            jnp.concatenate([-coupled[1], coupled[0]], 1),
        ],
        0,
    )
    reply = lax.dot_general(
        mixing,
        fields,
        (((0,), (0,)), ((), ())),
        precision=highest,
        preferred_element_type=jnp.float32,
    ).reshape(2, coupled.shape[2], -1)
    total = 0.0
    start = 0
    for part in portions:
        count = part.shape[1]
        piece = reply[:, start : start + count]
        total = total + jnp.sum(part[1] * piece[0] - part[0] * piece[1], axis=0)
        start += count
    return total


def layer(forward, backward, phase, footprint, groups):
    local_modes = backward.shape[1]
    pixel_count = backward.shape[2]
    phase_cos = jnp.cos(phase).reshape(pixel_count)
    phase_sin = jnp.sin(phase).reshape(pixel_count)

    def rotate(raw, cos=phase_cos, sin=phase_sin):
        return jnp.stack([raw[0] * cos - raw[1] * sin, raw[0] * sin + raw[1] * cos])

    split = local_modes // 2
    raw_first = shift_to(forward[:, :split], "blk", 2, 1)
    raw_second = shift_to(forward[:, split:], "blk", 2, 1)
    shifted = rotate(forward)
    tile_count = lax.axis_size(TILE)
    inverse_root = 1.0 / math.sqrt(pixel_count * tile_count)
    grad_scale = 0.25 / math.sqrt(MODES)
    column_share = MODES // tile_count
    me = lax.axis_index("blk")
    row_gate = jnp.repeat(footprint[:, 0].astype(jnp.float32), BLOCK)
    masked = backward * row_gate[None, :, None]
    fields = masked.reshape(2 * local_modes, pixel_count)

    own_groups = lax.dynamic_slice_in_dim(groups, me * local_modes, local_modes)
    other_groups = lax.dynamic_slice_in_dim(groups, (1 - me) * local_modes, local_modes)

    def coupled_of(margin_half, column_groups):
        weights = jnp.where(own_groups[:, None] == column_groups[None, :], 1.0, -cross_weight)
        return margin_half * weights.astype(jnp.float32)[None]

    own_block = pair_margin(fields, shifted)
    margin_own = tile_sum(own_block) * inverse_root
    sum_own = half_gradient(coupled_of(margin_own, own_groups), fields, [shifted])
    other_first = rotate(raw_first)
    first_block = pair_margin(fields, other_first)
    raw_second, sum_own, late_cos, late_sin = lax.optimization_barrier(
        (raw_second, sum_own, phase_cos, phase_sin)
    )
    other_second = rotate(raw_second, late_cos, late_sin)
    second_block = pair_margin(fields, other_second)
    first_front = tile_front(first_block.reshape(-1, split))
    fronts = [first_front, tile_front(second_block.reshape(-1, split))]
    part = fronts[0].shape[0]
    joined = tile_back(jnp.concatenate(fronts, 0))
    scattered = math.prod(size for _, size in SCATTERED)
    margin_other = (
        joined.reshape(scattered, 2, part, split)
        .transpose(1, 0, 2, 3)
        .reshape((2,) + first_block.shape)
        * inverse_root
    )
    sum_other = 0.0
    for index, portion in enumerate((other_first, other_second)):
        column_groups = lax.dynamic_slice_in_dim(other_groups, index * split, split)
        coupled = coupled_of(margin_other[index], column_groups)
        sum_other = sum_other + half_gradient(coupled, fields, [portion])

    column = lax.axis_index(TILE) * column_share
    offset = column % local_modes
    other_rows = lax.dynamic_index_in_dim(margin_other, offset // split, 0, keepdims=False)
    margin_out = jnp.where(
        column // local_modes == me,
        lax.dynamic_slice_in_dim(margin_own, offset, column_share, 2),
        lax.dynamic_slice_in_dim(other_rows, offset % split, column_share, 2),
    )

    local_sum = (sum_own + sum_other) * grad_scale
    half_width = pixel_count // 2
    keep = lax.dynamic_slice_in_dim(local_sum, me * half_width, half_width, 0)
    send = lax.dynamic_slice_in_dim(local_sum, (1 - me) * half_width, half_width, 0)
    gradient = keep + shift_to(send, "blk", 2, 1)
    return (margin_out, gradient.reshape(phase.shape[0], half_width))


def fine_mesh(mesh):
    devices = np.asarray(mesh.devices)
    blk, tile = devices.shape
    return jax.sharding.Mesh(devices.reshape(blk, 4, tile // 16, 2, 2), ("blk",) + TILE)


def solution(mesh):
    mesh = fine_mesh(mesh)
    placed = (
        P(None, "blk", TILE),
        P(None, "blk", TILE),
        P(TILE, None),
        P("blk", TILE),
        P(),
    )
    return jax.shard_map(
        layer,
        mesh=mesh,
        in_specs=placed,
        out_specs=(P(None, "blk", TILE), P(TILE, "blk")),
        check_vma=False,
    )
```

```python
import math

import jax
import jax.numpy as jnp
import numpy as np
from jax import lax
from jax.sharding import PartitionSpec as P


MODES = 1024
BLOCK = 64

TILE = ("z", "y", "xh", "core")
SCATTERED = (("core", 2), ("z", 4))
highest = lax.Precision.HIGH
cross_weight = 0.05


def shift_to(x, axis, size, step):
    return lax.ppermute(x, axis, [(j, (j + step) % size) for j in range(size)])


def scatter_rows(x, axis, size):
    me = lax.axis_index(axis)
    part = x.shape[0] // size
    total = lax.dynamic_slice_in_dim(x, me * part, part, 0)
    for step in range(1, size):
        send = lax.dynamic_slice_in_dim(x, ((me + step) % size) * part, part, 0)
        total = total + shift_to(send, axis, size, step)
    return total


def gather_rows(x, axis, size):
    me = lax.axis_index(axis)
    part = x.shape[0]
    out = jnp.zeros((size * part,) + x.shape[1:], x.dtype)
    out = lax.dynamic_update_slice_in_dim(out, x, me * part, 0)
    for step in range(1, size):
        got = shift_to(x, axis, size, step)
        out = lax.dynamic_update_slice_in_dim(out, got, ((me + size - step) % size) * part, 0)
    return out


def reduce_rows(x, axis, size):
    got = [shift_to(x, axis, size, step) for step in range(1, size)]
    for part in got:
        x = x + part
    return x


def tile_front(rows):
    for axis, size in SCATTERED:
        rows = scatter_rows(rows, axis, size)
    return reduce_rows(rows, "y", 4)


def tile_back(rows):
    rows = reduce_rows(rows, "xh", 2)
    for axis, size in reversed(SCATTERED):
        rows = gather_rows(rows, axis, size)
    return rows


def tile_sum(values):
    rows = values.reshape(-1, values.shape[-1])
    return tile_back(tile_front(rows)).reshape(values.shape)


def pair_margin(fields, portion):
    count = portion.shape[1]
    stacked = lax.dot_general(
        fields,
        portion.reshape(2 * count, -1),
        (((1,), (1,)), ((), ())),
        precision=highest,
        preferred_element_type=jnp.float32,
    )
    half = fields.shape[0] // 2
    real_part = stacked[:half, :count] + stacked[half:, count:]
    imag_part = stacked[:half, count:] - stacked[half:, :count]
    return jnp.stack([real_part, imag_part])


def half_gradient(coupled, fields, portions):
    mixing = jnp.concatenate(
        [
            jnp.concatenate([coupled[0], coupled[1]], 1),
            jnp.concatenate([-coupled[1], coupled[0]], 1),
        ],
        0,
    )
    reply = lax.dot_general(
        mixing,
        fields,
        (((0,), (0,)), ((), ())),
        precision=highest,
        preferred_element_type=jnp.float32,
    ).reshape(2, coupled.shape[2], -1)
    total = 0.0
    start = 0
    for part in portions:
        count = part.shape[1]
        piece = reply[:, start : start + count]
        total = total + jnp.sum(part[1] * piece[0] - part[0] * piece[1], axis=0)
        start += count
    return total


def layer(forward, backward, phase, footprint, groups):
    local_modes = backward.shape[1]
    pixel_count = backward.shape[2]
    phase_cos = jnp.cos(phase).reshape(pixel_count)
    phase_sin = jnp.sin(phase).reshape(pixel_count)

    def rotate(raw, cos=phase_cos, sin=phase_sin):
        return jnp.stack([raw[0] * cos - raw[1] * sin, raw[0] * sin + raw[1] * cos])

    split = local_modes // 2
    raw_first = shift_to(forward[:, :split], "blk", 2, 1)
    raw_second = shift_to(forward[:, split:], "blk", 2, 1)
    shifted = rotate(forward)
    tile_count = lax.axis_size(TILE)
    inverse_root = 1.0 / math.sqrt(pixel_count * tile_count)
    grad_scale = 0.25 / math.sqrt(MODES)
    column_share = MODES // tile_count
    me = lax.axis_index("blk")
    row_gate = jnp.repeat(footprint[:, 0].astype(jnp.float32), BLOCK)
    masked = backward * row_gate[None, :, None]
    fields = masked.reshape(2 * local_modes, pixel_count)

    own_groups = lax.dynamic_slice_in_dim(groups, me * local_modes, local_modes)
    other_groups = lax.dynamic_slice_in_dim(groups, (1 - me) * local_modes, local_modes)

    def coupled_of(margin_half, column_groups):
        weights = jnp.where(own_groups[:, None] == column_groups[None, :], 1.0, -cross_weight)
        return margin_half * weights.astype(jnp.float32)[None]

    own_block = pair_margin(fields, shifted)
    margin_own = tile_sum(own_block) * inverse_root
    sum_own = half_gradient(coupled_of(margin_own, own_groups), fields, [shifted])
    other_first = rotate(raw_first)
    first_block = pair_margin(fields, other_first)
    raw_second, sum_own, late_cos, late_sin = lax.optimization_barrier(
        (raw_second, sum_own, phase_cos, phase_sin)
    )
    other_second = rotate(raw_second, late_cos, late_sin)
    second_block = pair_margin(fields, other_second)
    first_front = tile_front(first_block.reshape(-1, split))
    fronts = [first_front, tile_front(second_block.reshape(-1, split))]
    part = fronts[0].shape[0]
    joined = tile_back(jnp.concatenate(fronts, 0))
    scattered = math.prod(size for _, size in SCATTERED)
    margin_other = (
        joined.reshape(scattered, 2, part, split)
        .transpose(1, 0, 2, 3)
        .reshape((2,) + first_block.shape)
        * inverse_root
    )
    other_margin = margin_other.transpose(1, 2, 0, 3).reshape(2, local_modes, local_modes)
    coupled = coupled_of(other_margin, other_groups)
    sum_other = half_gradient(coupled, fields, [other_first, other_second])

    column = lax.axis_index(TILE) * column_share
    offset = column % local_modes
    other_rows = lax.dynamic_index_in_dim(margin_other, offset // split, 0, keepdims=False)
    margin_out = jnp.where(
        column // local_modes == me,
        lax.dynamic_slice_in_dim(margin_own, offset, column_share, 2),
        lax.dynamic_slice_in_dim(other_rows, offset % split, column_share, 2),
    )

    local_sum = (sum_own + sum_other) * grad_scale
    half_width = pixel_count // 2
    keep = lax.dynamic_slice_in_dim(local_sum, me * half_width, half_width, 0)
    send = lax.dynamic_slice_in_dim(local_sum, (1 - me) * half_width, half_width, 0)
    gradient = keep + shift_to(send, "blk", 2, 1)
    return (margin_out, gradient.reshape(phase.shape[0], half_width))


def fine_mesh(mesh):
    devices = np.asarray(mesh.devices)
    blk, tile = devices.shape
    return jax.sharding.Mesh(devices.reshape(blk, 4, tile // 16, 2, 2), ("blk",) + TILE)


def solution(mesh):
    mesh = fine_mesh(mesh)
    placed = (
        P(None, "blk", TILE),
        P(None, "blk", TILE),
        P(TILE, None),
        P("blk", TILE),
        P(),
    )
    return jax.shard_map(
        layer,
        mesh=mesh,
        in_specs=placed,
        out_specs=(P(None, "blk", TILE), P(TILE, "blk")),
        check_vma=False,
    )
```

```python
import math

import jax
import jax.numpy as jnp
import numpy as np
from jax import lax
from jax.sharding import PartitionSpec as P


MODES = 1024
BLOCK = 64

TILE = ("z", "y", "xh", "core")
SCATTERED = (("core", 2), ("z", 4))
highest = lax.Precision.HIGH
cross_weight = 0.05


def shift_to(x, axis, size, step):
    return lax.ppermute(x, axis, [(j, (j + step) % size) for j in range(size)])


def scatter_rows(x, axis, size):
    me = lax.axis_index(axis)
    part = x.shape[0] // size
    total = lax.dynamic_slice_in_dim(x, me * part, part, 0)
    for step in range(1, size):
        send = lax.dynamic_slice_in_dim(x, ((me + step) % size) * part, part, 0)
        total = total + shift_to(send, axis, size, step)
    return total


def gather_rows(x, axis, size):
    me = lax.axis_index(axis)
    part = x.shape[0]
    out = jnp.zeros((size * part,) + x.shape[1:], x.dtype)
    out = lax.dynamic_update_slice_in_dim(out, x, me * part, 0)
    for step in range(1, size):
        got = shift_to(x, axis, size, step)
        out = lax.dynamic_update_slice_in_dim(out, got, ((me + size - step) % size) * part, 0)
    return out


def reduce_rows(x, axis, size):
    got = [shift_to(x, axis, size, step) for step in range(1, size)]
    for part in got:
        x = x + part
    return x


def tile_front(rows):
    for axis, size in SCATTERED:
        rows = scatter_rows(rows, axis, size)
    return reduce_rows(rows, "y", 4)


def tile_back(rows):
    rows = reduce_rows(rows, "xh", 2)
    for axis, size in reversed(SCATTERED):
        rows = gather_rows(rows, axis, size)
    return rows


def tile_sum(values):
    rows = values.reshape(-1, values.shape[-1])
    return tile_back(tile_front(rows)).reshape(values.shape)


def pair_margin(fields, portion):
    count = portion.shape[1]
    stacked = lax.dot_general(
        fields,
        portion.reshape(2 * count, -1),
        (((1,), (1,)), ((), ())),
        precision=highest,
        preferred_element_type=jnp.float32,
    )
    half = fields.shape[0] // 2
    real_part = stacked[:half, :count] + stacked[half:, count:]
    imag_part = stacked[:half, count:] - stacked[half:, :count]
    return jnp.stack([real_part, imag_part])


def half_gradient(coupled, fields, portions):
    mixing = jnp.concatenate(
        [
            jnp.concatenate([coupled[0], coupled[1]], 1),
            jnp.concatenate([-coupled[1], coupled[0]], 1),
        ],
        0,
    )
    reply = lax.dot_general(
        mixing,
        fields,
        (((0,), (0,)), ((), ())),
        precision=highest,
        preferred_element_type=jnp.float32,
    ).reshape(2, coupled.shape[2], -1)
    total = 0.0
    start = 0
    for part in portions:
        count = part.shape[1]
        piece = reply[:, start : start + count]
        total = total + jnp.sum(part[1] * piece[0] - part[0] * piece[1], axis=0)
        start += count
    return total


def layer(forward, backward, phase, footprint, groups):
    local_modes = backward.shape[1]
    pixel_count = backward.shape[2]
    phase_cos = jnp.cos(phase).reshape(pixel_count)
    phase_sin = jnp.sin(phase).reshape(pixel_count)

    def rotate(raw, cos=phase_cos, sin=phase_sin):
        return jnp.stack([raw[0] * cos - raw[1] * sin, raw[0] * sin + raw[1] * cos])

    split = local_modes * 3 // 4
    raw_first = shift_to(forward[:, :split], "blk", 2, 1)
    raw_second = shift_to(forward[:, split:], "blk", 2, 1)
    shifted = rotate(forward)
    tile_count = lax.axis_size(TILE)
    inverse_root = 1.0 / math.sqrt(pixel_count * tile_count)
    grad_scale = 0.25 / math.sqrt(MODES)
    column_share = MODES // tile_count
    me = lax.axis_index("blk")
    row_gate = jnp.repeat(footprint[:, 0].astype(jnp.float32), BLOCK)
    masked = backward * row_gate[None, :, None]
    fields = masked.reshape(2 * local_modes, pixel_count)

    own_groups = lax.dynamic_slice_in_dim(groups, me * local_modes, local_modes)
    other_groups = lax.dynamic_slice_in_dim(groups, (1 - me) * local_modes, local_modes)

    def coupled_of(margin_half, column_groups):
        weights = jnp.where(own_groups[:, None] == column_groups[None, :], 1.0, -cross_weight)
        return margin_half * weights.astype(jnp.float32)[None]

    own_block = pair_margin(fields, shifted)
    margin_own = tile_sum(own_block) * inverse_root
    sum_own = half_gradient(coupled_of(margin_own, own_groups), fields, [shifted])
    other_first = rotate(raw_first)
    first_block = pair_margin(fields, other_first)
    raw_second, sum_own, late_cos, late_sin = lax.optimization_barrier(
        (raw_second, sum_own, phase_cos, phase_sin)
    )
    other_second = rotate(raw_second, late_cos, late_sin)
    second_block = pair_margin(fields, other_second)
    lanes = 128
    first_front = tile_front(first_block.reshape(-1, lanes))
    fronts = [first_front, tile_front(second_block.reshape(-1, lanes))]
    cut = fronts[0].shape[0]
    joined = tile_back(jnp.concatenate(fronts, 0))
    scattered = math.prod(size for _, size in SCATTERED)
    joined = joined.reshape(scattered, -1, lanes)
    first_margin = joined[:, :cut].reshape(first_block.shape) * inverse_root
    second_margin = joined[:, cut:].reshape(second_block.shape) * inverse_root
    sum_other = 0.0
    pieces = ((first_margin, other_first, 0), (second_margin, other_second, split))
    for margin_piece, portion, start in pieces:
        count = portion.shape[1]
        column_groups = lax.dynamic_slice_in_dim(other_groups, start, count)
        coupled = coupled_of(margin_piece, column_groups)
        sum_other = sum_other + half_gradient(coupled, fields, [portion])

    column = lax.axis_index(TILE) * column_share
    offset = column % local_modes
    in_first = offset < split
    from_first = lax.dynamic_slice_in_dim(
        first_margin, jnp.minimum(offset, split - column_share), column_share, 2
    )
    from_second = lax.dynamic_slice_in_dim(
        second_margin, jnp.maximum(offset - split, 0), column_share, 2
    )
    margin_out = jnp.where(
        column // local_modes == me,
        lax.dynamic_slice_in_dim(margin_own, offset, column_share, 2),
        jnp.where(in_first, from_first, from_second),
    )

    local_sum = (sum_own + sum_other) * grad_scale
    half_width = pixel_count // 2
    keep = lax.dynamic_slice_in_dim(local_sum, me * half_width, half_width, 0)
    send = lax.dynamic_slice_in_dim(local_sum, (1 - me) * half_width, half_width, 0)
    gradient = keep + shift_to(send, "blk", 2, 1)
    return (margin_out, gradient.reshape(phase.shape[0], half_width))


def fine_mesh(mesh):
    devices = np.asarray(mesh.devices)
    blk, tile = devices.shape
    return jax.sharding.Mesh(devices.reshape(blk, 4, tile // 16, 2, 2), ("blk",) + TILE)


def solution(mesh):
    mesh = fine_mesh(mesh)
    placed = (
        P(None, "blk", TILE),
        P(None, "blk", TILE),
        P(TILE, None),
        P("blk", TILE),
        P(),
    )
    return jax.shard_map(
        layer,
        mesh=mesh,
        in_specs=placed,
        out_specs=(P(None, "blk", TILE), P(TILE, "blk")),
        check_vma=False,
    )
```

```python
import math

import jax
import jax.numpy as jnp
import numpy as np
from jax import lax
from jax.sharding import PartitionSpec as P


MODES = 1024
BLOCK = 64

TILE = ("z", "y", "xh", "core")
SCATTERED = (("core", 2), ("z", 4))
highest = lax.Precision.HIGH
cross_weight = 0.05


def shift_to(x, axis, size, step):
    return lax.ppermute(x, axis, [(j, (j + step) % size) for j in range(size)])


def scatter_rows(x, axis, size):
    me = lax.axis_index(axis)
    part = x.shape[0] // size
    total = lax.dynamic_slice_in_dim(x, me * part, part, 0)
    for step in range(1, size):
        send = lax.dynamic_slice_in_dim(x, ((me + step) % size) * part, part, 0)
        total = total + shift_to(send, axis, size, step)
    return total


def gather_rows(x, axis, size):
    me = lax.axis_index(axis)
    part = x.shape[0]
    out = jnp.zeros((size * part,) + x.shape[1:], x.dtype)
    out = lax.dynamic_update_slice_in_dim(out, x, me * part, 0)
    for step in range(1, size):
        got = shift_to(x, axis, size, step)
        out = lax.dynamic_update_slice_in_dim(out, got, ((me + size - step) % size) * part, 0)
    return out


def reduce_rows(x, axis, size):
    got = [shift_to(x, axis, size, step) for step in range(1, size)]
    for part in got:
        x = x + part
    return x


def tile_front(rows):
    for axis, size in SCATTERED:
        rows = scatter_rows(rows, axis, size)
    return reduce_rows(rows, "y", 4)


def tile_back(rows):
    rows = reduce_rows(rows, "xh", 2)
    for axis, size in reversed(SCATTERED):
        rows = gather_rows(rows, axis, size)
    return rows


def tile_sum(values):
    rows = values.reshape(-1, values.shape[-1])
    return tile_back(tile_front(rows)).reshape(values.shape)


def pair_margin(fields, portion):
    count = portion.shape[1]
    stacked = lax.dot_general(
        fields,
        portion.reshape(2 * count, -1),
        (((1,), (1,)), ((), ())),
        precision=highest,
        preferred_element_type=jnp.float32,
    )
    half = fields.shape[0] // 2
    real_part = stacked[:half, :count] + stacked[half:, count:]
    imag_part = stacked[:half, count:] - stacked[half:, :count]
    return jnp.stack([real_part, imag_part])


def half_gradient(coupled, fields, portions):
    mixing = jnp.concatenate(
        [
            jnp.concatenate([coupled[0], coupled[1]], 1),
            jnp.concatenate([-coupled[1], coupled[0]], 1),
        ],
        0,
    )
    reply = lax.dot_general(
        mixing,
        fields,
        (((0,), (0,)), ((), ())),
        precision=highest,
        preferred_element_type=jnp.float32,
    ).reshape(2, coupled.shape[2], -1)
    total = 0.0
    start = 0
    for part in portions:
        count = part.shape[1]
        piece = reply[:, start : start + count]
        total = total + jnp.sum(part[1] * piece[0] - part[0] * piece[1], axis=0)
        start += count
    return total


def layer(forward, backward, phase, footprint, groups):
    local_modes = backward.shape[1]
    pixel_count = backward.shape[2]
    phase_cos = jnp.cos(phase).reshape(pixel_count)
    phase_sin = jnp.sin(phase).reshape(pixel_count)

    def rotate(raw, cos=phase_cos, sin=phase_sin):
        return jnp.stack([raw[0] * cos - raw[1] * sin, raw[0] * sin + raw[1] * cos])

    split = local_modes // 2
    raw_first = shift_to(forward[:, :split], "blk", 2, 1)
    raw_second = shift_to(forward[:, split:], "blk", 2, 1)
    shifted = rotate(forward)
    tile_count = lax.axis_size(TILE)
    inverse_root = 1.0 / math.sqrt(pixel_count * tile_count)
    grad_scale = 0.25 / math.sqrt(MODES)
    column_share = MODES // tile_count
    me = lax.axis_index("blk")
    row_gate = jnp.repeat(footprint[:, 0].astype(jnp.float32), BLOCK)
    masked = backward * row_gate[None, :, None]
    fields = masked.reshape(2 * local_modes, pixel_count)

    own_groups = lax.dynamic_slice_in_dim(groups, me * local_modes, local_modes)
    other_groups = lax.dynamic_slice_in_dim(groups, (1 - me) * local_modes, local_modes)

    def coupled_of(margin_half, column_groups):
        weights = jnp.where(own_groups[:, None] == column_groups[None, :], 1.0, -cross_weight)
        return margin_half * weights.astype(jnp.float32)[None]

    own_block = pair_margin(fields, shifted)
    margin_own = tile_sum(own_block) * inverse_root
    sum_own = half_gradient(coupled_of(margin_own, own_groups), fields, [shifted])
    other_first = rotate(raw_first)
    first_block = pair_margin(fields, other_first)
    raw_second, sum_own, late_cos, late_sin = lax.optimization_barrier(
        (raw_second, sum_own, phase_cos, phase_sin)
    )
    other_second = rotate(raw_second, late_cos, late_sin)
    second_block = pair_margin(fields, other_second)
    first_front = tile_front(first_block.reshape(-1, split))
    first_margin = tile_back(first_front).reshape(first_block.shape)
    second_margin = tile_back(tile_front(second_block.reshape(-1, split))).reshape(second_block.shape)
    margin_other = jnp.stack([first_margin, second_margin]) * inverse_root
    sum_other = 0.0
    for index, portion in enumerate((other_first, other_second)):
        column_groups = lax.dynamic_slice_in_dim(other_groups, index * split, split)
        coupled = coupled_of(margin_other[index], column_groups)
        sum_other = sum_other + half_gradient(coupled, fields, [portion])

    column = lax.axis_index(TILE) * column_share
    offset = column % local_modes
    other_rows = lax.dynamic_index_in_dim(margin_other, offset // split, 0, keepdims=False)
    margin_out = jnp.where(
        column // local_modes == me,
        lax.dynamic_slice_in_dim(margin_own, offset, column_share, 2),
        lax.dynamic_slice_in_dim(other_rows, offset % split, column_share, 2),
    )

    local_sum = (sum_own + sum_other) * grad_scale
    half_width = pixel_count // 2
    keep = lax.dynamic_slice_in_dim(local_sum, me * half_width, half_width, 0)
    send = lax.dynamic_slice_in_dim(local_sum, (1 - me) * half_width, half_width, 0)
    gradient = keep + shift_to(send, "blk", 2, 1)
    return (margin_out, gradient.reshape(phase.shape[0], half_width))


def fine_mesh(mesh):
    devices = np.asarray(mesh.devices)
    blk, tile = devices.shape
    return jax.sharding.Mesh(devices.reshape(blk, 4, tile // 16, 2, 2), ("blk",) + TILE)


def solution(mesh):
    mesh = fine_mesh(mesh)
    placed = (
        P(None, "blk", TILE),
        P(None, "blk", TILE),
        P(TILE, None),
        P("blk", TILE),
        P(),
    )
    return jax.shard_map(
        layer,
        mesh=mesh,
        in_specs=placed,
        out_specs=(P(None, "blk", TILE), P(TILE, "blk")),
        check_vma=False,
    )
```

```python
import math

import jax
import jax.numpy as jnp
import numpy as np
from jax import lax
from jax.sharding import PartitionSpec as P


MODES = 1024
BLOCK = 64

TILE = ("z", "y", "xh", "core")
SCATTERED = (("core", 2), ("z", 4))
highest = lax.Precision.HIGH
cross_weight = 0.05


def shift_to(x, axis, size, step):
    return lax.ppermute(x, axis, [(j, (j + step) % size) for j in range(size)])


def scatter_rows(x, axis, size):
    me = lax.axis_index(axis)
    part = x.shape[0] // size
    total = lax.dynamic_slice_in_dim(x, me * part, part, 0)
    for step in range(1, size):
        send = lax.dynamic_slice_in_dim(x, ((me + step) % size) * part, part, 0)
        total = total + shift_to(send, axis, size, step)
    return total


def gather_rows(x, axis, size):
    me = lax.axis_index(axis)
    part = x.shape[0]
    out = jnp.zeros((size * part,) + x.shape[1:], x.dtype)
    out = lax.dynamic_update_slice_in_dim(out, x, me * part, 0)
    for step in range(1, size):
        got = shift_to(x, axis, size, step)
        out = lax.dynamic_update_slice_in_dim(out, got, ((me + size - step) % size) * part, 0)
    return out


def reduce_rows(x, axis, size):
    got = [shift_to(x, axis, size, step) for step in range(1, size)]
    for part in got:
        x = x + part
    return x


def tile_front(rows):
    for axis, size in SCATTERED:
        rows = scatter_rows(rows, axis, size)
    return reduce_rows(rows, "y", 4)


def tile_back(rows):
    rows = reduce_rows(rows, "xh", 2)
    for axis, size in reversed(SCATTERED):
        rows = gather_rows(rows, axis, size)
    return rows


def tile_sum(values):
    rows = values.reshape(-1, values.shape[-1])
    return tile_back(tile_front(rows)).reshape(values.shape)


def pair_margin(fields, portion):
    count = portion.shape[1]
    stacked = lax.dot_general(
        fields,
        portion.reshape(2 * count, -1),
        (((1,), (1,)), ((), ())),
        precision=highest,
        preferred_element_type=jnp.float32,
    )
    half = fields.shape[0] // 2
    real_part = stacked[:half, :count] + stacked[half:, count:]
    imag_part = stacked[:half, count:] - stacked[half:, :count]
    return jnp.stack([real_part, imag_part])


def half_gradient(coupled, fields, portions):
    mixing = jnp.concatenate(
        [
            jnp.concatenate([coupled[0], coupled[1]], 1),
            jnp.concatenate([-coupled[1], coupled[0]], 1),
        ],
        0,
    )
    reply = lax.dot_general(
        mixing,
        fields,
        (((0,), (0,)), ((), ())),
        precision=highest,
        preferred_element_type=jnp.float32,
    ).reshape(2, coupled.shape[2], -1)
    total = 0.0
    start = 0
    for part in portions:
        count = part.shape[1]
        piece = reply[:, start : start + count]
        total = total + jnp.sum(part[1] * piece[0] - part[0] * piece[1], axis=0)
        start += count
    return total


def layer(forward, backward, phase, footprint, groups):
    local_modes = backward.shape[1]
    pixel_count = backward.shape[2]
    phase_cos = jnp.cos(phase).reshape(pixel_count)
    phase_sin = jnp.sin(phase).reshape(pixel_count)

    def rotate(raw, cos=phase_cos, sin=phase_sin):
        return jnp.stack([raw[0] * cos - raw[1] * sin, raw[0] * sin + raw[1] * cos])

    split = local_modes // 2
    raw_first = shift_to(forward[:, :split], "blk", 2, 1)
    raw_second = shift_to(forward[:, split:], "blk", 2, 1)
    shifted = rotate(forward)
    tile_count = lax.axis_size(TILE)
    inverse_root = 1.0 / math.sqrt(pixel_count * tile_count)
    grad_scale = 0.25 / math.sqrt(MODES)
    column_share = MODES // tile_count
    me = lax.axis_index("blk")
    row_gate = jnp.repeat(footprint[:, 0].astype(jnp.float32), BLOCK)
    masked = backward * row_gate[None, :, None]
    fields = masked.reshape(2 * local_modes, pixel_count)

    own_groups = lax.dynamic_slice_in_dim(groups, me * local_modes, local_modes)
    other_groups = lax.dynamic_slice_in_dim(groups, (1 - me) * local_modes, local_modes)

    def coupled_of(margin_half, column_groups, row_groups=own_groups):
        weights = jnp.where(row_groups[:, None] == column_groups[None, :], 1.0, -cross_weight)
        return margin_half * weights.astype(jnp.float32)[None]

    own_block = pair_margin(fields, shifted)
    margin_own = tile_sum(own_block) * inverse_root
    sum_own = half_gradient(coupled_of(margin_own, own_groups), fields, [shifted])
    other_first = rotate(raw_first)
    first_block = pair_margin(fields, other_first)
    raw_second, sum_own, late_cos, late_sin = lax.optimization_barrier(
        (raw_second, sum_own, phase_cos, phase_sin)
    )
    other_second = rotate(raw_second, late_cos, late_sin)
    second_block = pair_margin(fields, other_second)
    first_front = tile_front(first_block.reshape(-1, split))
    first_margin = tile_back(first_front).reshape(first_block.shape)
    second_front = tile_front(second_block.reshape(-1, split))
    second_margin = tile_back(second_front).reshape(second_block.shape)
    margin_other = (first_margin * inverse_root, second_margin * inverse_root)
    sum_other = 0.0
    late_fields, late_groups, late_margin = lax.optimization_barrier(
        (fields, own_groups, margin_other[1])
    )
    margin_other = (margin_other[0], late_margin)
    for index, portion in enumerate((other_first, other_second)):
        column_groups = lax.dynamic_slice_in_dim(other_groups, index * split, split)
        coupled = coupled_of(margin_other[index], column_groups, (own_groups, late_groups)[index])
        sum_other = sum_other + half_gradient(coupled, (fields, late_fields)[index], [portion])

    column = lax.axis_index(TILE) * column_share
    offset = column % local_modes
    other_slices = [
        lax.dynamic_slice_in_dim(rows, offset % split, column_share, 2) for rows in margin_other
    ]
    margin_out = jnp.where(
        column // local_modes == me,
        lax.dynamic_slice_in_dim(margin_own, offset, column_share, 2),
        jnp.where(offset // split == 0, other_slices[0], other_slices[1]),
    )

    local_sum = (sum_own + sum_other) * grad_scale
    half_width = pixel_count // 2
    keep = lax.dynamic_slice_in_dim(local_sum, me * half_width, half_width, 0)
    send = lax.dynamic_slice_in_dim(local_sum, (1 - me) * half_width, half_width, 0)
    gradient = keep + shift_to(send, "blk", 2, 1)
    return (margin_out, gradient.reshape(phase.shape[0], half_width))


def fine_mesh(mesh):
    devices = np.asarray(mesh.devices)
    blk, tile = devices.shape
    return jax.sharding.Mesh(devices.reshape(blk, 4, tile // 16, 2, 2), ("blk",) + TILE)


def solution(mesh):
    mesh = fine_mesh(mesh)
    placed = (
        P(None, "blk", TILE),
        P(None, "blk", TILE),
        P(TILE, None),
        P("blk", TILE),
        P(),
    )
    return jax.shard_map(
        layer,
        mesh=mesh,
        in_specs=placed,
        out_specs=(P(None, "blk", TILE), P(TILE, "blk")),
        check_vma=False,
    )
```
